512 devices in a mesh: exp: 128 (over y, z, core), hid: 4 (over x).
Axes of the slice: x: 4, y: 8, z: 8, core: 2. Of those that a mesh axis runs over, the one named last changes fastest.
Arguments:
- tokens: bfloat16 [4096, 4096], P('exp', 'hid'), may hold values from -6 to 6
- expert_ids: int32 [4096, 8], P('exp'), may hold values from 0 to 127, all different within a row; in each aligned block of 16 rows (0 to 15, 16 to 31, ...) at most 2 rows name the same one
- combine: float32 [4096, 8], P('exp'), may hold values from 0.05 to 0.4
- sign_bits: int32 [128, 768], P('exp'), may hold values from 0 to 1
- w_gate: bfloat16 [128, 768, 4096], P('exp', 'hid'), may hold values from -0.09375 to 0.09375
- w_up: bfloat16 [128, 768, 4096], P('exp', 'hid'), may hold values from -0.09375 to 0.09375
- w_down: bfloat16 [128, 768, 4096], P('exp', 'hid'), may hold values from -0.21875 to 0.21875
Outputs:
- next_input: bfloat16 [4096, 4096], P('exp', 'hid')
- hessian: bfloat16 [128, 768, 768], P('exp', 'hid')
The draws below stay inside these ranges and needn't reach their ends.
Inputs may be any that keep to these rules, and one draw needn't show every extreme that they name: `expert_ids`: each row names 8 different experts. Within each aligned block of 16 rows (one micro-batch of one index of exp) no expert is named by more than 2 rows, a bound that some block reaches. `sign_bits`: 0 stands for the sign -1, 1 for +1.
All inputs are finite; a program needn't handle non-finite values.
Results may differ from the reference program's by a relative error of at most 0.0065.
Values may be sent and summed in bfloat16 or wider, within the bound.
No kernel may reach another device: no remote copies, remote signals or barrier semaphores. Data moves between devices by JAX's collectives and lax.ppermute only.
A program may use at most 64 MiB of HBM per device.

```python
import math
import jax
import jax.numpy as jnp
import numpy as np
from jax import lax

D = 4096
TOP = 8
SYL = 64
FFE = 768
EXPERTS = 128
HALF = 16
CAP = 2
TOKENS = 4096
N_EXP = 128
N_HID = 4


def with_ends(values, key, smallest, top_value):
    longest = values.shape.index(max(values.shape))
    spots = []
    for shift in (0, 1):
        where = [jax.random.randint(jax.random.fold_in(key, axis), (), 0, length) for axis, length in enumerate(values.shape)]
        where[longest] = (where[longest] + shift) % values.shape[longest]
        spots.append(tuple(where))
    return values.at[spots[0]].set(smallest).at[spots[1]].set(top_value)


def shard_levels(key, shape, pieces, least, largest):
    gain = 1.0
    for position, blocks in pieces:
        draws = jax.random.uniform(jax.random.fold_in(jax.random.fold_in(key, 6), position), (blocks,), jnp.float32, least / len(pieces), largest / len(pieces))
        gain = gain * jnp.repeat(jnp.exp(draws), shape[position] // blocks).reshape((-1,) + (1,) * (len(shape) - 1 - position))
    return gain


def shared_out(stream_key, own, number, rows, number_of, top, limit, lean):
    ranking = jax.random.permutation(stream_key, number_of)
    heavy_load, usual = portions_of(number_of, rows * top, limit, lean, True), portions_of(number_of, rows * top, limit, lean, False)
    places = jnp.arange(number_of)

    def named(tallies, rotation):
        used = int((tallies > 0).sum())
        fixed = max(1, used // 4)
        passed = fixed + (places - fixed + rotation * (used - fixed)) % max(1, number_of - fixed)
        return jnp.zeros((number_of,), jnp.int32).at[ranking[jnp.where(places < fixed, places, passed)]].set(jnp.asarray(tallies, jnp.int32))

    tallies = jnp.where(number % 4 == 0, named(heavy_load, number // 4), named(usual, number - number // 4 - 1))
    mixed = jax.random.permutation(jax.random.fold_in(own, 3), number_of)
    donor, sink = mixed[0:number_of // 2 * 2:2], mixed[1:number_of // 2 * 2:2]
    margin = jnp.minimum(tallies[donor] - 1, limit - tallies[sink]) // 2
    margin = jnp.where((donor == ranking[0]) | (sink == ranking[0]) | (tallies[sink] == 0), 0, jnp.maximum(margin, 0))
    passed = jax.random.randint(jax.random.fold_in(own, 4), (number_of // 2,), 0, 1 << 20) % (margin + 1)
    tallies = tallies.at[donor].add(-passed).at[sink].add(passed)
    members = jnp.searchsorted(jnp.cumsum(tallies), jnp.arange(rows * top), side="right").astype(jnp.int32)
    listing = members.reshape(top, rows).T
    listing = listing[jax.random.permutation(jax.random.fold_in(own, 1), rows)]
    rotation = jax.random.randint(jax.random.fold_in(own, 2), (rows, 1), 0, top)
    return jnp.take_along_axis(listing, (jnp.arange(top)[None, :] + rotation) % top, axis=1)


def portions_of(count, total, reach, lean, full):
    portions = [(1 << 20) // math.isqrt(grade ** lean) + 1 for grade in range(1, count + 1)]
    largest = reach if full else min(reach, max(-(-total // count), total * portions[0] // sum(portions)))
    least = 1 if total - largest >= count - 1 else 0
    holding, surplus = [largest] + [least] * (count - 1), total - largest - least * (count - 1)
    while surplus > 0:
        free = [i for i in range(1, count) if holding[i] < largest] or [i for i in range(1, count) if holding[i] < reach]
        pool, left = sum([portions[i] for i in free]), surplus
        for i in free:
            addition = min(reach - holding[i], max(1, left * portions[i] // pool), surplus)
            holding[i] = holding[i] + addition
            surplus = surplus - addition
    return np.array(holding)


def gaussian(rng, extent, deviation, bound, split=(), held_as=jnp.bfloat16):
    drawn = deviation * jax.random.normal(rng, extent, jnp.float32)
    if split:
        drawn = drawn * shard_levels(rng, extent, split, -0.22, 0.18)
    return jnp.clip(drawn, -bound, bound).astype(held_as)


def setup_inputs(seed: int = 0) -> dict:
    streams_of = jax.random.split(jax.random.key(seed), 8)
    tokens = gaussian(streams_of[0], (TOKENS, D), 1.0, 6.0, ((0, 128), (1, 4)))
    expert_ids_keys = jax.random.split(jax.random.fold_in(streams_of[1], 1), TOKENS // HALF)
    expert_ids_turns = jax.random.permutation(jax.random.fold_in(streams_of[1], 3), TOKENS // HALF)
    expert_ids = jax.vmap(lambda own, number: shared_out(jax.random.fold_in(streams_of[1], 2), own, number, HALF, EXPERTS, TOP, CAP, 2))(expert_ids_keys, expert_ids_turns).reshape((TOKENS, TOP))
    combine = jnp.clip(jnp.exp(math.log(0.4) - 2.0794415 * jax.random.uniform(streams_of[2], (TOKENS, TOP), jnp.float32) ** shard_levels(streams_of[2], (TOKENS, TOP), ((0, 128),), -0.2, 0.2)), 0.05, 0.4)
    sign_bits = with_ends(jax.random.randint(streams_of[3], (EXPERTS, FFE), 0, 2), jax.random.fold_in(streams_of[3], 1), 0, 1).astype(jnp.int32)
    w_gate = gaussian(streams_of[4], (EXPERTS, FFE, D), D ** -0.5, 0.09375, ((0, 128), (1, 4)))
    w_up = gaussian(streams_of[5], (EXPERTS, FFE, D), D ** -0.5, 0.09375, ((0, 128), (1, 4)))
    w_down = gaussian(streams_of[6], (EXPERTS, FFE, D), FFE ** -0.5, 0.21875, ((0, 128), (1, 4)))
    return {"tokens": tokens, "expert_ids": expert_ids, "combine": combine, "sign_bits": sign_bits, "w_gate": w_gate, "w_up": w_up, "w_down": w_down}


def paley_twelve():
    residues = set((number * number) % 11 for number in range(1, 11))
    legendre = [0] + [1 if number in residues else -1 for number in range(1, 11)]
    hadamard = np.zeros((12, 12))
    hadamard[0, 1:] = 1.0
    hadamard[1:, 0] = -1.0
    for row_index in range(11):
        for col_index in range(11):
            hadamard[row_index + 1, col_index + 1] = legendre[(col_index - row_index) % 11]
    return hadamard + np.eye(12)


def sylvester(order_size):
    positions = jnp.arange(order_size, dtype=jnp.int32)
    common = positions[:, None] & positions[None, :]
    parity = jnp.zeros_like(common)
    for bit_pos in range(order_size.bit_length()):
        parity = parity + ((common >> bit_pos) & 1)
    return (1 - 2 * (parity % 2)).astype(jnp.float32)


def rotate(hidden, sign_rows, paley_table, sylvester_table):
    values = hidden.astype(jnp.float32) * jnp.expand_dims(sign_rows, -2)
    blocks = values.reshape(values.shape[:-1] + (12, sylvester_table.shape[0]))
    turned = jnp.einsum("...ab,ca,db->...cd", blocks, paley_table, sylvester_table,
                        precision=lax.Precision.HIGHEST)
    return turned.reshape(values.shape)


def rank_of_pick(ids_block):
    flat_ids = ids_block.reshape(-1)
    onehot = (flat_ids[:, None] == jnp.arange(EXPERTS, dtype=jnp.int32)[None, :]).astype(jnp.int32)
    before = jnp.cumsum(onehot, axis=0) - onehot
    return jnp.sum(before * onehot, axis=1).reshape(ids_block.shape)


def reference(tokens, expert_ids, combine, sign_bits, w_gate, w_up, w_down):
    paley_table = jnp.asarray(paley_twelve(), jnp.float32)
    sylvester_table = sylvester(SYL)
    slot_count = N_EXP * CAP
    sign_all = (2 * sign_bits - 1).astype(jnp.float32)
    gram_total = jnp.zeros((EXPERTS, FFE, FFE), jnp.float32)
    blocks_ids = expert_ids.reshape(N_EXP, 2, HALF, TOP)
    blocks_tok = tokens.reshape(N_EXP, 2, HALF, D)
    blocks_comb = combine.reshape(N_EXP, 2, HALF, TOP)
    results = []
    for batch_index in range(2):
        ids_now = blocks_ids[:, batch_index]
        ranks_now = jax.vmap(rank_of_pick)(ids_now)
        source = jnp.arange(N_EXP, dtype=jnp.int32)[:, None, None]
        row_pos = source * CAP + ranks_now
        token_pos = source * HALF + jnp.arange(HALF, dtype=jnp.int32)[None, :, None] + jnp.zeros_like(ids_now)
        owner_row = jnp.full((EXPERTS, slot_count), -1, jnp.int32)
        owner_row = owner_row.at[ids_now.reshape(-1), row_pos.reshape(-1)].set(token_pos.reshape(-1))
        tok_now = blocks_tok[:, batch_index].reshape(N_EXP * HALF, D)

        def one_expert(packed):
            owner_e, weight_gate, weight_up, weight_down, sign_row = packed
            expert_in = jnp.where(owner_e[:, None] >= 0, tok_now[jnp.maximum(owner_e, 0)],
                                  jnp.zeros((), jnp.bfloat16))
            gate_act = jnp.dot(expert_in, weight_gate.T, preferred_element_type=jnp.float32)
            up_act = jnp.dot(expert_in, weight_up.T, preferred_element_type=jnp.float32)
            hidden = (jax.nn.silu(gate_act) * up_act).astype(jnp.bfloat16)
            partial_value = jnp.einsum("sjf,jfd->jsd",
                                 hidden.reshape(slot_count, N_HID, FFE // N_HID).astype(jnp.float32),
                                 weight_down.reshape(N_HID, FFE // N_HID, D).astype(jnp.float32))
            partial_value = lax.optimization_barrier(partial_value.astype(jnp.bfloat16)).astype(jnp.float32)
            expert_out = jnp.sum(partial_value, axis=0).astype(jnp.bfloat16)
            rotated = rotate(hidden, sign_row, paley_table, sylvester_table)
            gram = jnp.dot(rotated.T, rotated, precision=lax.Precision.HIGHEST)
            return expert_out, gram

        outs_now, gram_now = lax.map(one_expert, (owner_row, w_gate, w_up, w_down, sign_all))
        gram_total = gram_total + gram_now
        gathered = outs_now[ids_now, row_pos]
        mixed_rows = blocks_tok[:, batch_index].astype(jnp.float32) + jnp.sum(
            blocks_comb[:, batch_index][..., None] * gathered.astype(jnp.float32), axis=2)
        results.append(mixed_rows.astype(jnp.bfloat16))
    next_input = jnp.stack(results, axis=1).reshape(TOKENS, D)
    gram_scale = EXPERTS / (TOKENS * TOP * FFE)
    hessian = (gram_total * gram_scale).astype(jnp.bfloat16)
    return next_input, hessian
```

```python
import jax
import jax.numpy as jnp
import numpy as np
from jax import lax
from jax.sharding import PartitionSpec as P


def paley_twelve():
    residues = set((number * number % 11 for number in range(1, 11)))
    legendre = [0] + [1 if number in residues else -1 for number in range(1, 11)]
    hadamard = np.zeros((12, 12))
    hadamard[0, 1:] = 1.0
    hadamard[1:, 0] = -1.0
    for row_index in range(11):
        for col_index in range(11):
            hadamard[row_index + 1, col_index + 1] = legendre[(col_index - row_index) % 11]
    return hadamard + np.eye(12)


def sylvester(order_size):
    positions = jnp.arange(order_size, dtype=jnp.int32)
    common = positions[:, None] & positions[None, :]
    parity = jnp.zeros_like(common)
    for bit_pos in range(order_size.bit_length()):
        parity = parity + (common >> bit_pos & 1)
    return (1 - 2 * (parity % 2)).astype(jnp.float32)


def rotate(hidden, sign_rows, paley_table, sylvester_table):
    values = hidden.astype(jnp.float32) * jnp.expand_dims(sign_rows, -2)
    blocks = values.reshape(values.shape[:-1] + (12, sylvester_table.shape[0]))
    turned = jnp.einsum(
        "...ab,ca,db->...cd", blocks, paley_table, sylvester_table, precision=lax.Precision.HIGHEST
    )
    return turned.reshape(values.shape)


def rank_of_pick(ids_block, experts):
    flat_ids = ids_block.reshape(-1)
    onehot = (flat_ids[:, None] == jnp.arange(experts, dtype=jnp.int32)[None, :]).astype(jnp.int32)
    before = jnp.cumsum(onehot, axis=0) - onehot
    return jnp.sum(before * onehot, axis=1).reshape(ids_block.shape)


def local(tokens, expert_ids, combine, sign_bits, w_gate, w_up, w_down):
    n_exp = lax.axis_size("exp")
    n_hid = lax.axis_size("hid")
    hid_index = lax.axis_index("hid")
    local_experts = w_gate.shape[0]
    experts = local_experts * n_exp
    tok_rows = tokens.shape[0]
    half_rows = tok_rows // 2
    top_count = expert_ids.shape[1]
    capacity = min(half_rows, max(2, 2 * half_rows * top_count // experts))
    hidden_units = sign_bits.shape[1]
    share_rows = hidden_units // n_hid
    slot_count = n_exp * capacity
    paley_table = jnp.asarray(paley_twelve(), jnp.float32)
    sylvester_table = sylvester(hidden_units // 12)
    sign_rows = (2 * sign_bits - 1).astype(jnp.float32)
    gram_scale = experts / (tok_rows * n_exp * top_count * hidden_units)
    down_cols = lax.all_to_all(w_down, "hid", split_axis=2, concat_axis=1, tiled=True)
    gram_total = jnp.zeros((local_experts, share_rows, hidden_units), jnp.float32)
    results = []
    for batch_index in range(2):
        first_row = batch_index * half_rows
        ids_block = expert_ids[first_row : first_row + half_rows]
        picks_rank = rank_of_pick(ids_block, experts)
        target = ids_block * capacity + picks_rank
        selector = jnp.any(
            target[None, :, :] == jnp.arange(experts * capacity, dtype=jnp.int32)[:, None, None],
            axis=2,
        ).astype(jnp.bfloat16)
        sending = jnp.dot(
            selector,
            tokens[first_row : first_row + half_rows],
            preferred_element_type=jnp.float32,
        ).astype(jnp.bfloat16)
        arrived = lax.all_to_all(sending, "exp", split_axis=0, concat_axis=0, tiled=True)
        arrived = lax.all_gather(arrived, "hid", axis=1, tiled=True)
        row_width = arrived.shape[1]
        expert_in = arrived.reshape(n_exp, local_experts, capacity, row_width).transpose(1, 0, 2, 3)
        expert_in = expert_in.reshape(local_experts, slot_count, row_width)
        gate_act = jnp.einsum("esd,efd->esf", expert_in, w_gate, preferred_element_type=jnp.float32)
        up_act = jnp.einsum("esd,efd->esf", expert_in, w_up, preferred_element_type=jnp.float32)
        hidden = (jax.nn.silu(gate_act) * up_act).astype(jnp.bfloat16)
        full_hidden = lax.all_gather(hidden, "hid", axis=2, tiled=True)
        summed = jnp.einsum(
            "esf,efd->esd", full_hidden, down_cols, preferred_element_type=jnp.float32
        ).astype(jnp.bfloat16)
        outgoing = summed.reshape(local_experts, n_exp, capacity, -1).transpose(1, 0, 2, 3)
        outgoing = outgoing.reshape(n_exp * local_experts * capacity, -1)
        back_rows = lax.all_to_all(outgoing, "exp", split_axis=0, concat_axis=0, tiled=True)
        picked = back_rows[target]
        weights = combine[first_row : first_row + half_rows]
        mixed_rows = tokens[first_row : first_row + half_rows].astype(jnp.float32) + jnp.sum(
            weights[:, :, None] * picked.astype(jnp.float32), axis=1
        )
        results.append(mixed_rows.astype(jnp.bfloat16))
        rotated = rotate(full_hidden, sign_rows, paley_table, sylvester_table)
        own_rotated = lax.dynamic_slice_in_dim(rotated, hid_index * share_rows, share_rows, 2)
        gram_total = gram_total + jnp.einsum(
            "esi,esj->eij", own_rotated, rotated, precision=lax.Precision.HIGHEST
        )
    hessian = (gram_total * gram_scale).astype(jnp.bfloat16)
    return (jnp.concatenate(results, axis=0), hessian)


def solution(mesh):
    placed = (
        P("exp", "hid"),
        P("exp", None),
        P("exp", None),
        P("exp", None),
        P("exp", "hid", None),
        P("exp", "hid", None),
        P("exp", "hid", None),
    )
    return jax.shard_map(
        local,
        mesh=mesh,
        in_specs=placed,
        out_specs=(P("exp", "hid"), P("exp", "hid", None)),
        check_vma=False,
    )
```

```python
import jax
import jax.numpy as jnp
import numpy as np
from jax import lax
from jax.sharding import PartitionSpec as P


def paley_twelve():
    residues = set((number * number % 11 for number in range(1, 11)))
    legendre = [0] + [1 if number in residues else -1 for number in range(1, 11)]
    hadamard = np.zeros((12, 12))
    hadamard[0, 1:] = 1.0
    hadamard[1:, 0] = -1.0
    for row_index in range(11):
        for col_index in range(11):
            hadamard[row_index + 1, col_index + 1] = legendre[(col_index - row_index) % 11]
    return hadamard + np.eye(12)


def sylvester(order_size):
    positions = jnp.arange(order_size, dtype=jnp.int32)
    common = positions[:, None] & positions[None, :]
    parity = jnp.zeros_like(common)
    for bit_pos in range(order_size.bit_length()):
        parity = parity + (common >> bit_pos & 1)
    return (1 - 2 * (parity % 2)).astype(jnp.float32)


def rotate(hidden, sign_rows, paley_table, sylvester_table):
    values = hidden.astype(jnp.float32) * jnp.expand_dims(sign_rows, -2)
    blocks = values.reshape(values.shape[:-1] + (12, sylvester_table.shape[0]))
    turned = jnp.einsum(
        "...ab,ca,db->...cd", blocks, paley_table, sylvester_table, precision=lax.Precision.HIGHEST
    )
    return turned.reshape(values.shape)


def rank_of_pick(ids_block, experts):
    flat_ids = ids_block.reshape(-1)
    onehot = (flat_ids[:, None] == jnp.arange(experts, dtype=jnp.int32)[None, :]).astype(jnp.int32)
    before = jnp.cumsum(onehot, axis=0) - onehot
    return jnp.sum(before * onehot, axis=1).reshape(ids_block.shape)


def local(tokens, expert_ids, combine, sign_bits, w_gate, w_up, w_down):
    n_exp = lax.axis_size("exp")
    n_hid = lax.axis_size("hid")
    hid_index = lax.axis_index("hid")
    experts = w_gate.shape[0] * n_exp
    tok_rows, own_cols = tokens.shape
    half_rows = tok_rows // 2
    top_count = expert_ids.shape[1]
    capacity = min(half_rows, max(2, 2 * half_rows * top_count // experts))
    hidden_units = sign_bits.shape[1]
    share_rows = hidden_units // n_hid
    per_pair = 2 * capacity
    paley_table = jnp.asarray(paley_twelve(), jnp.float32)
    sylvester_table = sylvester(hidden_units // 12)
    sign_rows = (2 * sign_bits - 1).astype(jnp.float32)
    gram_scale = experts / (tok_rows * n_exp * top_count * hidden_units)
    down_parts = w_down[0].reshape(share_rows, n_hid, own_cols).transpose(1, 0, 2)
    down_cols = lax.all_to_all(down_parts, "hid", split_axis=0, concat_axis=0, tiled=True)
    down_cols = down_cols.reshape(hidden_units, own_cols)
    ranks = jnp.concatenate(
        [rank_of_pick(expert_ids[b * half_rows : (b + 1) * half_rows], experts) for b in range(2)],
        axis=0,
    )
    batch_of_row = (jnp.arange(tok_rows, dtype=jnp.int32) // half_rows)[:, None]
    target = expert_ids * per_pair + batch_of_row * capacity + ranks
    selector = jnp.any(
        target[None, :, :] == jnp.arange(experts * per_pair, dtype=jnp.int32)[:, None, None],
        axis=2,
    ).astype(jnp.bfloat16)
    sending = jnp.dot(selector, tokens, preferred_element_type=jnp.float32).astype(jnp.bfloat16)
    arrived = lax.all_to_all(sending, "exp", split_axis=0, concat_axis=0, tiled=True)
    expert_in = lax.all_gather(arrived, "hid", axis=1, tiled=True)
    gate_act = jnp.dot(expert_in, w_gate[0].T, preferred_element_type=jnp.float32)
    up_act = jnp.dot(expert_in, w_up[0].T, preferred_element_type=jnp.float32)
    hidden = (jax.nn.silu(gate_act) * up_act).astype(jnp.bfloat16)
    full_hidden = lax.all_gather(hidden, "hid", axis=1, tiled=True)
    out_cols = jnp.dot(full_hidden, down_cols, preferred_element_type=jnp.float32).astype(
        jnp.bfloat16
    )
    back_rows = lax.all_to_all(out_cols, "exp", split_axis=0, concat_axis=0, tiled=True)
    picked = back_rows[target]
    mixed_rows = tokens.astype(jnp.float32) + jnp.sum(
        combine[:, :, None] * picked.astype(jnp.float32), axis=1
    )
    rotated = rotate(full_hidden, sign_rows[0], paley_table, sylvester_table)
    own_rotated = lax.dynamic_slice_in_dim(rotated, hid_index * share_rows, share_rows, 1)
    gram = jnp.dot(own_rotated.T, rotated, precision=lax.Precision.HIGHEST)
    hessian = (gram * gram_scale).astype(jnp.bfloat16)
    return (mixed_rows.astype(jnp.bfloat16), hessian[None])


def solution(mesh):
    placed = (
        P("exp", "hid"),
        P("exp", None),
        P("exp", None),
        P("exp", None),
        P("exp", "hid", None),
        P("exp", "hid", None),
        P("exp", "hid", None),
    )
    return jax.shard_map(
        local,
        mesh=mesh,
        in_specs=placed,
        out_specs=(P("exp", "hid"), P("exp", "hid", None)),
        check_vma=False,
    )
```

```python
import jax
import jax.numpy as jnp
import numpy as np
from jax import lax
from jax.sharding import PartitionSpec as P


def paley_twelve():
    residues = set((number * number % 11 for number in range(1, 11)))
    legendre = [0] + [1 if number in residues else -1 for number in range(1, 11)]
    hadamard = np.zeros((12, 12))
    hadamard[0, 1:] = 1.0
    hadamard[1:, 0] = -1.0
    for row_index in range(11):
        for col_index in range(11):
            hadamard[row_index + 1, col_index + 1] = legendre[(col_index - row_index) % 11]
    return hadamard + np.eye(12)


def sylvester(order_size):
    positions = jnp.arange(order_size, dtype=jnp.int32)
    common = positions[:, None] & positions[None, :]
    parity = jnp.zeros_like(common)
    for bit_pos in range(order_size.bit_length()):
        parity = parity + (common >> bit_pos & 1)
    return (1 - 2 * (parity % 2)).astype(jnp.float32)


def rotate(hidden, sign_rows, paley_table, sylvester_table):
    values = hidden.astype(jnp.float32) * jnp.expand_dims(sign_rows, -2)
    blocks = values.reshape(values.shape[:-1] + (12, sylvester_table.shape[0]))
    turned = jnp.einsum(
        "...ab,ca,db->...cd", blocks, paley_table, sylvester_table, precision=lax.Precision.HIGHEST
    )
    return turned.reshape(values.shape)


def rank_of_pick(ids_block, experts):
    flat_ids = ids_block.reshape(-1)
    onehot = (flat_ids[:, None] == jnp.arange(experts, dtype=jnp.int32)[None, :]).astype(jnp.int32)
    before = jnp.cumsum(onehot, axis=0) - onehot
    return jnp.sum(before * onehot, axis=1).reshape(ids_block.shape)


def shift_hid(value, shift, n_hid):
    return lax.ppermute(value, "hid", [(i, (i + shift) % n_hid) for i in range(n_hid)])


def local(tokens, expert_ids, combine, sign_bits, w_gate, w_up, w_down):
    n_exp = lax.axis_size("exp")
    n_hid = lax.axis_size("hid")
    hid_index = lax.axis_index("hid")
    experts = w_gate.shape[0] * n_exp
    tok_rows, own_cols = tokens.shape
    half_rows = tok_rows // 2
    top_count = expert_ids.shape[1]
    capacity = min(half_rows, max(2, 2 * half_rows * top_count // experts))
    hidden_units = sign_bits.shape[1]
    share_rows = hidden_units // n_hid
    per_pair = 2 * capacity
    paley_table = jnp.asarray(paley_twelve(), jnp.float32)
    sylvester_table = sylvester(hidden_units // 12)
    sign_rows = (2 * sign_bits - 1).astype(jnp.float32)
    gram_scale = experts / (tok_rows * n_exp * top_count * hidden_units)
    shifts = range(n_hid)
    source = [(hid_index - s) % n_hid for s in shifts]
    down_pieces = [
        shift_hid(
            lax.dynamic_slice_in_dim(w_down[0], ((hid_index + s) % n_hid) * own_cols, own_cols, 1),
            s,
            n_hid,
        )
        if s
        else lax.dynamic_slice_in_dim(w_down[0], hid_index * own_cols, own_cols, 1)
        for s in shifts
    ]
    ranks = jnp.concatenate(
        [rank_of_pick(expert_ids[b * half_rows : (b + 1) * half_rows], experts) for b in range(2)],
        axis=0,
    )
    batch_of_row = (jnp.arange(tok_rows, dtype=jnp.int32) // half_rows)[:, None]
    target = expert_ids * per_pair + batch_of_row * capacity + ranks
    selector = jnp.any(
        target[None, :, :] == jnp.arange(experts * per_pair, dtype=jnp.int32)[:, None, None],
        axis=2,
    ).astype(jnp.bfloat16)
    sending = jnp.dot(selector, tokens, preferred_element_type=jnp.float32).astype(jnp.bfloat16)
    arrived = lax.all_to_all(sending, "exp", split_axis=0, concat_axis=0, tiled=True)
    in_pieces = [shift_hid(arrived, s, n_hid) if s else arrived for s in shifts]
    gate_act = sum(
        jnp.dot(
            in_pieces[s],
            lax.dynamic_slice_in_dim(w_gate[0], source[s] * own_cols, own_cols, 1).T,
            preferred_element_type=jnp.float32,
        )
        for s in shifts
    )
    up_act = sum(
        jnp.dot(
            in_pieces[s],
            lax.dynamic_slice_in_dim(w_up[0], source[s] * own_cols, own_cols, 1).T,
            preferred_element_type=jnp.float32,
        )
        for s in shifts
    )
    hidden = (jax.nn.silu(gate_act) * up_act).astype(jnp.bfloat16)
    hid_pieces = [shift_hid(hidden, s, n_hid) if s else hidden for s in shifts]
    out_cols = sum(
        jnp.dot(hid_pieces[s], down_pieces[s], preferred_element_type=jnp.float32) for s in shifts
    ).astype(jnp.bfloat16)
    back_rows = lax.all_to_all(out_cols, "exp", split_axis=0, concat_axis=0, tiled=True)
    picked = back_rows[target]
    mixed_rows = tokens.astype(jnp.float32) + jnp.sum(
        combine[:, :, None] * picked.astype(jnp.float32), axis=1
    )
    stacked = jnp.stack(hid_pieces)
    order = (hid_index - jnp.arange(n_hid, dtype=jnp.int32)) % n_hid
    full_hidden = jnp.take(stacked, order, axis=0).transpose(1, 0, 2).reshape(-1, hidden_units)
    rotated = rotate(full_hidden, sign_rows[0], paley_table, sylvester_table)
    own_rotated = lax.dynamic_slice_in_dim(rotated, hid_index * share_rows, share_rows, 1)
    gram = jnp.dot(own_rotated.T, rotated, precision=lax.Precision.HIGHEST)
    hessian = (gram * gram_scale).astype(jnp.bfloat16)
    return (mixed_rows.astype(jnp.bfloat16), hessian[None])


def solution(mesh):
    placed = (
        P("exp", "hid"),
        P("exp", None),
        P("exp", None),
        P("exp", None),
        P("exp", "hid", None),
        P("exp", "hid", None),
        P("exp", "hid", None),
    )
    return jax.shard_map(
        local,
        mesh=mesh,
        in_specs=placed,
        out_specs=(P("exp", "hid"), P("exp", "hid", None)),
        check_vma=False,
    )
```

```python
import jax
import jax.numpy as jnp
import numpy as np
from jax import lax
from jax.sharding import PartitionSpec as P


def paley_twelve():
    residues = set((number * number % 11 for number in range(1, 11)))
    legendre = [0] + [1 if number in residues else -1 for number in range(1, 11)]
    hadamard = np.zeros((12, 12))
    hadamard[0, 1:] = 1.0
    hadamard[1:, 0] = -1.0
    for row_index in range(11):
        for col_index in range(11):
            hadamard[row_index + 1, col_index + 1] = legendre[(col_index - row_index) % 11]
    return hadamard + np.eye(12)


def sylvester(order_size):
    positions = jnp.arange(order_size, dtype=jnp.int32)
    common = positions[:, None] & positions[None, :]
    parity = jnp.zeros_like(common)
    for bit_pos in range(order_size.bit_length()):
        parity = parity + (common >> bit_pos & 1)
    return (1 - 2 * (parity % 2)).astype(jnp.float32)


def rotate(hidden, sign_rows, paley_table, sylvester_table):
    values = hidden.astype(jnp.float32) * jnp.expand_dims(sign_rows, -2)
    blocks = values.reshape(values.shape[:-1] + (12, sylvester_table.shape[0]))
    turned = jnp.einsum(
        "...ab,ca,db->...cd", blocks, paley_table, sylvester_table, precision=lax.Precision.HIGHEST
    )
    return turned.reshape(values.shape)


def rank_of_pick(ids_block, experts):
    flat_ids = ids_block.reshape(-1)
    onehot = (flat_ids[:, None] == jnp.arange(experts, dtype=jnp.int32)[None, :]).astype(jnp.int32)
    before = jnp.cumsum(onehot, axis=0) - onehot
    return jnp.sum(before * onehot, axis=1).reshape(ids_block.shape)


def shift_hid(value, shift, n_hid):
    return lax.ppermute(value, "hid", [(i, (i + shift) % n_hid) for i in range(n_hid)])


def layer(tokens, expert_ids, combine, sign_bits, w_gate, w_up, w_down):
    n_exp = lax.axis_size("exp")
    n_hid = lax.axis_size("hid")
    hid_index = lax.axis_index("hid")
    experts = w_gate.shape[0] * n_exp
    tok_rows, own_cols = tokens.shape
    half_rows = tok_rows // 2
    top_count = expert_ids.shape[1]
    capacity = min(half_rows, max(2, 2 * half_rows * top_count // experts))
    hidden_units = sign_bits.shape[1]
    share_rows = hidden_units // n_hid
    per_pair = 2 * capacity
    paley_table = jnp.asarray(paley_twelve(), jnp.float32)
    sylvester_table = sylvester(hidden_units // 12)
    sign_rows = (2 * sign_bits - 1).astype(jnp.float32)
    gram_scale = experts / (tok_rows * n_exp * top_count * hidden_units)
    shifts = range(n_hid)
    source = [(hid_index - s) % n_hid for s in shifts]
    down_send = [
        lax.dynamic_slice_in_dim(w_down[0], ((hid_index + s) % n_hid) * own_cols, own_cols, 1)
        for s in shifts
    ]
    ranks = jnp.concatenate(
        [rank_of_pick(expert_ids[b * half_rows : (b + 1) * half_rows], experts) for b in range(2)],
        axis=0,
    )
    batch_of_row = (jnp.arange(tok_rows, dtype=jnp.int32) // half_rows)[:, None]
    target = expert_ids * per_pair + batch_of_row * capacity + ranks
    selector = jnp.any(
        target[None, :, :] == jnp.arange(experts * per_pair, dtype=jnp.int32)[:, None, None],
        axis=2,
    ).astype(jnp.bfloat16)
    sending = jnp.dot(selector, tokens, preferred_element_type=jnp.float32).astype(jnp.bfloat16)
    arrived = lax.all_to_all(sending, "exp", split_axis=0, concat_axis=0, tiled=True)
    slot_rows = arrived.shape[0]
    both = [
        shift_hid(jnp.concatenate([arrived, down_send[s]], axis=0), s, n_hid) if s else None
        for s in shifts
    ]
    in_pieces = [both[s][:slot_rows] if s else arrived for s in shifts]
    down_pieces = [both[s][slot_rows:] if s else down_send[0] for s in shifts]
    gate_act = sum(
        jnp.dot(
            in_pieces[s],
            lax.dynamic_slice_in_dim(w_gate[0], source[s] * own_cols, own_cols, 1).T,
            preferred_element_type=jnp.float32,
        )
        for s in shifts
    )
    up_act = sum(
        jnp.dot(
            in_pieces[s],
            lax.dynamic_slice_in_dim(w_up[0], source[s] * own_cols, own_cols, 1).T,
            preferred_element_type=jnp.float32,
        )
        for s in shifts
    )
    hidden = (jax.nn.silu(gate_act) * up_act).astype(jnp.bfloat16)
    hid_pieces = [shift_hid(hidden, s, n_hid) if s else hidden for s in shifts]
    out_cols = sum(
        jnp.dot(hid_pieces[s], down_pieces[s], preferred_element_type=jnp.float32) for s in shifts
    ).astype(jnp.bfloat16)
    back_rows = lax.all_to_all(out_cols, "exp", split_axis=0, concat_axis=0, tiled=True)
    picked = back_rows[target]
    mixed_rows = tokens.astype(jnp.float32) + jnp.sum(
        combine[:, :, None] * picked.astype(jnp.float32), axis=1
    )
    stacked = jnp.stack(hid_pieces)
    order = (hid_index - jnp.arange(n_hid, dtype=jnp.int32)) % n_hid
    full_hidden = jnp.take(stacked, order, axis=0).transpose(1, 0, 2).reshape(-1, hidden_units)
    rotated = rotate(full_hidden, sign_rows[0], paley_table, sylvester_table)
    own_rotated = lax.dynamic_slice_in_dim(rotated, hid_index * share_rows, share_rows, 1)
    gram = jnp.dot(own_rotated.T, rotated, precision=lax.Precision.HIGHEST)
    hessian = (gram * gram_scale).astype(jnp.bfloat16)
    return (mixed_rows.astype(jnp.bfloat16), hessian[None])


def solution(mesh):
    placed = (
        P("exp", "hid"),
        P("exp", None),
        P("exp", None),
        P("exp", None),
        P("exp", "hid", None),
        P("exp", "hid", None),
        P("exp", "hid", None),
    )
    return jax.shard_map(
        layer,
        mesh=mesh,
        in_specs=placed,
        out_specs=(P("exp", "hid"), P("exp", "hid", None)),
        check_vma=False,
    )
```

```python
import jax
import jax.numpy as jnp
import numpy as np
from jax import lax
from jax.sharding import PartitionSpec as P


def paley_twelve():
    residues = set((number * number % 11 for number in range(1, 11)))
    legendre = [0] + [1 if number in residues else -1 for number in range(1, 11)]
    hadamard = np.zeros((12, 12))
    hadamard[0, 1:] = 1.0
    hadamard[1:, 0] = -1.0
    for row_index in range(11):
        for col_index in range(11):
            hadamard[row_index + 1, col_index + 1] = legendre[(col_index - row_index) % 11]
    return hadamard + np.eye(12)


def sylvester(order_size):
    positions = jnp.arange(order_size, dtype=jnp.int32)
    common = positions[:, None] & positions[None, :]
    parity = jnp.zeros_like(common)
    for bit_pos in range(order_size.bit_length()):
        parity = parity + (common >> bit_pos & 1)
    return (1 - 2 * (parity % 2)).astype(jnp.float32)


def rotate(hidden, sign_rows, paley_table, sylvester_table):
    values = hidden.astype(jnp.float32) * jnp.expand_dims(sign_rows, -2)
    blocks = values.reshape(values.shape[:-1] + (12, sylvester_table.shape[0]))
    turned = jnp.einsum(
        "...ab,ca,db->...cd", blocks, paley_table, sylvester_table, precision=lax.Precision.HIGHEST
    )
    return turned.reshape(values.shape)


def rank_of_pick(ids_block, experts):
    flat_ids = ids_block.reshape(-1)
    onehot = (flat_ids[:, None] == jnp.arange(experts, dtype=jnp.int32)[None, :]).astype(jnp.int32)
    before = jnp.cumsum(onehot, axis=0) - onehot
    return jnp.sum(before * onehot, axis=1).reshape(ids_block.shape)


def shift_hid(value, shift, n_hid):
    return lax.ppermute(value, "hid", [(i, (i + shift) % n_hid) for i in range(n_hid)])


def layer(tokens, expert_ids, combine, sign_bits, w_gate, w_up, w_down):
    n_exp = lax.axis_size("exp")
    n_hid = lax.axis_size("hid")
    hid_index = lax.axis_index("hid")
    experts = w_gate.shape[0] * n_exp
    tok_rows, own_cols = tokens.shape
    half_rows = tok_rows // 2
    top_count = expert_ids.shape[1]
    capacity = min(half_rows, max(2, 2 * half_rows * top_count // experts))
    hidden_units = sign_bits.shape[1]
    share_rows = hidden_units // n_hid
    per_pair = 2 * capacity
    paley_table = jnp.asarray(paley_twelve(), jnp.float32)
    sylvester_table = sylvester(hidden_units // 12)
    sign_rows = (2 * sign_bits - 1).astype(jnp.float32)
    gram_scale = experts / (tok_rows * n_exp * top_count * hidden_units)
    shifts = range(n_hid)
    source = [(hid_index - s) % n_hid for s in shifts]
    down_pieces = [
        shift_hid(
            lax.dynamic_slice_in_dim(w_down[0], ((hid_index + s) % n_hid) * own_cols, own_cols, 1),
            s,
            n_hid,
        )
        if s
        else lax.dynamic_slice_in_dim(w_down[0], hid_index * own_cols, own_cols, 1)
        for s in shifts
    ]
    ranks = jnp.concatenate(
        [rank_of_pick(expert_ids[b * half_rows : (b + 1) * half_rows], experts) for b in range(2)],
        axis=0,
    )
    batch_of_row = (jnp.arange(tok_rows, dtype=jnp.int32) // half_rows)[:, None]
    target = expert_ids * per_pair + batch_of_row * capacity + ranks
    selector = jnp.any(
        target[None, :, :] == jnp.arange(experts * per_pair, dtype=jnp.int32)[:, None, None],
        axis=2,
    ).astype(jnp.bfloat16)
    sending = jnp.dot(selector, tokens, preferred_element_type=jnp.float32).astype(jnp.bfloat16)
    arrived = lax.all_to_all(sending, "exp", split_axis=0, concat_axis=0, tiled=True)
    in_pieces = [arrived]
    for s in shifts[1:]:
        in_pieces.append(shift_hid(arrived, s, n_hid))
    gate_act = sum(
        jnp.dot(
            in_pieces[s],
            lax.dynamic_slice_in_dim(w_gate[0], source[s] * own_cols, own_cols, 1).T,
            preferred_element_type=jnp.float32,
        )
        for s in shifts
    )
    up_act = sum(
        jnp.dot(
            in_pieces[s],
            lax.dynamic_slice_in_dim(w_up[0], source[s] * own_cols, own_cols, 1).T,
            preferred_element_type=jnp.float32,
        )
        for s in shifts
    )
    hidden = (jax.nn.silu(gate_act) * up_act).astype(jnp.bfloat16)
    hid_pieces = [shift_hid(hidden, s, n_hid) if s else hidden for s in shifts]
    out_cols = sum(
        jnp.dot(hid_pieces[s], down_pieces[s], preferred_element_type=jnp.float32) for s in shifts
    ).astype(jnp.bfloat16)
    back_rows = lax.all_to_all(out_cols, "exp", split_axis=0, concat_axis=0, tiled=True)
    picked = back_rows[target]
    mixed_rows = tokens.astype(jnp.float32) + jnp.sum(
        combine[:, :, None] * picked.astype(jnp.float32), axis=1
    )
    stacked = jnp.stack(hid_pieces)
    order = (hid_index - jnp.arange(n_hid, dtype=jnp.int32)) % n_hid
    full_hidden = jnp.take(stacked, order, axis=0).transpose(1, 0, 2).reshape(-1, hidden_units)
    rotated = rotate(full_hidden, sign_rows[0], paley_table, sylvester_table)
    own_rotated = lax.dynamic_slice_in_dim(rotated, hid_index * share_rows, share_rows, 1)
    gram = jnp.dot(own_rotated.T, rotated, precision=lax.Precision.HIGHEST)
    hessian = (gram * gram_scale).astype(jnp.bfloat16)
    return (mixed_rows.astype(jnp.bfloat16), hessian[None])


def solution(mesh):
    placed = (
        P("exp", "hid"),
        P("exp", None),
        P("exp", None),
        P("exp", None),
        P("exp", "hid", None),
        P("exp", "hid", None),
        P("exp", "hid", None),
    )
    return jax.shard_map(
        layer,
        mesh=mesh,
        in_specs=placed,
        out_specs=(P("exp", "hid"), P("exp", "hid", None)),
        check_vma=False,
    )
```

```python
import jax
import jax.numpy as jnp
import numpy as np
from jax import lax
from jax.sharding import PartitionSpec as P


def paley_twelve():
    residues = set((number * number % 11 for number in range(1, 11)))
    legendre = [0] + [1 if number in residues else -1 for number in range(1, 11)]
    hadamard = np.zeros((12, 12))
    hadamard[0, 1:] = 1.0
    hadamard[1:, 0] = -1.0
    for row_index in range(11):
        for col_index in range(11):
            hadamard[row_index + 1, col_index + 1] = legendre[(col_index - row_index) % 11]
    return hadamard + np.eye(12)


def sylvester(order_size):
    positions = jnp.arange(order_size, dtype=jnp.int32)
    common = positions[:, None] & positions[None, :]
    parity = jnp.zeros_like(common)
    for bit_pos in range(order_size.bit_length()):
        parity = parity + (common >> bit_pos & 1)
    return (1 - 2 * (parity % 2)).astype(jnp.float32)


def rotate(hidden, sign_rows, paley_table, sylvester_table):
    values = hidden.astype(jnp.float32) * jnp.expand_dims(sign_rows, -2)
    blocks = values.reshape(values.shape[:-1] + (12, sylvester_table.shape[0]))
    turned = jnp.einsum(
        "...ab,ca,db->...cd", blocks, paley_table, sylvester_table, precision=lax.Precision.HIGHEST
    )
    return turned.reshape(values.shape)


def rank_of_pick(ids_block, experts):
    flat_ids = ids_block.reshape(-1)
    onehot = (flat_ids[:, None] == jnp.arange(experts, dtype=jnp.int32)[None, :]).astype(jnp.int32)
    before = jnp.cumsum(onehot, axis=0) - onehot
    return jnp.sum(before * onehot, axis=1).reshape(ids_block.shape)


def shift_hid(value, shift, n_hid):
    return lax.ppermute(value, "hid", [(i, (i + shift) % n_hid) for i in range(n_hid)])


def layer(tokens, expert_ids, combine, sign_bits, w_gate, w_up, w_down):
    n_exp = lax.axis_size("exp")
    n_hid = lax.axis_size("hid")
    hid_index = lax.axis_index("hid")
    experts = w_gate.shape[0] * n_exp
    tok_rows, own_cols = tokens.shape
    half_rows = tok_rows // 2
    top_count = expert_ids.shape[1]
    capacity = min(half_rows, max(2, 2 * half_rows * top_count // experts))
    hidden_units = sign_bits.shape[1]
    share_rows = hidden_units // n_hid
    per_pair = 2 * capacity
    paley_table = jnp.asarray(paley_twelve(), jnp.float32)
    sylvester_table = sylvester(hidden_units // 12)
    sign_rows = (2 * sign_bits - 1).astype(jnp.float32)
    gram_scale = experts / (tok_rows * n_exp * top_count * hidden_units)
    shifts = range(n_hid)
    source = [(hid_index - s) % n_hid for s in shifts]
    down_pieces = [
        shift_hid(
            lax.dynamic_slice_in_dim(w_down[0], ((hid_index + s) % n_hid) * own_cols, own_cols, 1),
            s,
            n_hid,
        )
        if s
        else lax.dynamic_slice_in_dim(w_down[0], hid_index * own_cols, own_cols, 1)
        for s in shifts
    ]
    ranks = jnp.concatenate(
        [rank_of_pick(expert_ids[b * half_rows : (b + 1) * half_rows], experts) for b in range(2)],
        axis=0,
    )
    batch_of_row = (jnp.arange(tok_rows, dtype=jnp.int32) // half_rows)[:, None]
    target = expert_ids * per_pair + batch_of_row * capacity + ranks
    selector = jnp.any(
        target[None, :, :] == jnp.arange(experts * per_pair, dtype=jnp.int32)[:, None, None],
        axis=2,
    ).astype(jnp.bfloat16)
    sending = jnp.dot(selector, tokens, preferred_element_type=jnp.float32).astype(jnp.bfloat16)
    arrived = lax.all_to_all(sending, "exp", split_axis=0, concat_axis=0, tiled=True)
    in_pieces = [shift_hid(arrived, s, n_hid) if s else arrived for s in shifts]
    gate_act = sum(
        jnp.dot(
            in_pieces[s],
            lax.dynamic_slice_in_dim(w_gate[0], source[s] * own_cols, own_cols, 1).T,
            preferred_element_type=jnp.float32,
        )
        for s in shifts
    )
    up_act = sum(
        jnp.dot(
            in_pieces[s],
            lax.dynamic_slice_in_dim(w_up[0], source[s] * own_cols, own_cols, 1).T,
            preferred_element_type=jnp.float32,
        )
        for s in shifts
    )
    hidden = (jax.nn.silu(gate_act) * up_act).astype(jnp.bfloat16)
    hid_pieces = [shift_hid(hidden, s, n_hid) if s else hidden for s in shifts]
    out_cols = sum(
        jnp.dot(hid_pieces[s], down_pieces[s], preferred_element_type=jnp.float32) for s in shifts
    ).astype(jnp.bfloat16)
    out_cols = out_cols.reshape(n_exp, per_pair, own_cols)
    back_rows = lax.all_to_all(out_cols, "exp", split_axis=0, concat_axis=0, tiled=True)
    picked = back_rows[target // per_pair, target % per_pair]
    mixed_rows = tokens.astype(jnp.float32) + jnp.sum(
        combine[:, :, None] * picked.astype(jnp.float32), axis=1
    )
    stacked = jnp.stack(hid_pieces)
    order = (hid_index - jnp.arange(n_hid, dtype=jnp.int32)) % n_hid
    full_hidden = jnp.take(stacked, order, axis=0).transpose(1, 0, 2).reshape(-1, hidden_units)
    rotated = rotate(full_hidden, sign_rows[0], paley_table, sylvester_table)
    own_rotated = lax.dynamic_slice_in_dim(rotated, hid_index * share_rows, share_rows, 1)
    gram = jnp.dot(own_rotated.T, rotated, precision=lax.Precision.HIGHEST)
    hessian = (gram * gram_scale).astype(jnp.bfloat16)
    return (mixed_rows.astype(jnp.bfloat16), hessian[None])


def solution(mesh):
    placed = (
        P("exp", "hid"),
        P("exp", None),
        P("exp", None),
        P("exp", None),
        P("exp", "hid", None),
        P("exp", "hid", None),
        P("exp", "hid", None),
    )
    return jax.shard_map(
        layer,
        mesh=mesh,
        in_specs=placed,
        out_specs=(P("exp", "hid"), P("exp", "hid", None)),
        check_vma=False,
    )
```
